256 devices in a mesh: cx: 16 (over x, y), cy: 16 (over z, core).
Axes of the slice: x: 4, y: 4, z: 8, core: 2. Of those that a mesh axis runs over, the one named last changes fastest.
Arguments:
- query_rows: bfloat16 [65536, 1024], P(('cx', 'cy')), may hold values from -6 to 6
- key_rows: bfloat16 [65536, 1024], P(('cx', 'cy')), may hold values from -6 to 6
- value_rows: bfloat16 [65536, 1024], P(('cx', 'cy')), may hold values from -6 to 6
- forward_out: bfloat16 [65536, 1024], P(('cx', 'cy')), may hold values from -6 to 6
- out_grad: bfloat16 [65536, 1024], P(('cx', 'cy')), may hold values from -6 to 6
- doc_blocks: int32 [64], replicated, may hold values from 1 to 15, 512 in all
Outputs:
- query_grad: bfloat16 [65536, 1024], P(('cx', 'cy'))
- key_grad: bfloat16 [65536, 1024], P(('cx', 'cy'))
- value_grad: bfloat16 [65536, 1024], P(('cx', 'cy'))
The draws below stay inside these ranges and needn't reach their ends.
Inputs may be any that keep to these rules, and one draw needn't show every extreme that they name: `doc_blocks`: lengths of the documents in blocks of 128 tokens, in sequence order, summing to 512; the longest has exactly 15 blocks.
All inputs are finite; a program needn't handle non-finite values.
Results may differ from the reference program's by a relative error of at most 0.0049.
Values may be sent and summed in bfloat16 or wider, within the bound.
No kernel may reach another device: no remote copies, remote signals or barrier semaphores. Data moves between devices by JAX's collectives and lax.ppermute only.
A program may use at most 128 MiB of HBM per device.

```python
import math
import jax
import jax.numpy as jnp
import numpy as np
from jax import lax

HEADS = 8
DH = 128
TOK_DEV = 256
BLOCK = 128
REACH = 7
TOKENS = 65536
MOST_BLOCKS = 15
NDOC = 64


def drawn_pair(key):
    shape = (TOKENS, HEADS * DH)
    queries = jax.random.normal(jax.random.fold_in(key, 11), shape, jnp.float32)
    keys_out = jax.random.normal(jax.random.fold_in(key, 12), shape, jnp.float32)
    return (jnp.clip(queries, -6.0, 6.0), jnp.clip(keys_out, -6.0, 6.0))


def draw_query_rows(key, part):
    return drawn_pair(key)[0].astype(jnp.bfloat16)


def draw_key_rows(key, part):
    return drawn_pair(key)[1].astype(jnp.bfloat16)


def level_of(rng, shape, split, smallest, top_value):
    factor_of = 1.0
    for dim, parts in split:
        draws = jax.random.uniform(jax.random.fold_in(jax.random.fold_in(rng, 6), dim), (parts,), jnp.float32, smallest / len(split), top_value / len(split))
        factor_of = factor_of * jnp.repeat(jnp.exp(draws), shape[dim] // parts).reshape((-1,) + (1,) * (len(shape) - 1 - dim))
    return factor_of


def profile(count, total, reach, lean):
    loads = [(1 << 20) // math.isqrt(rank ** lean) + 1 for rank in range(2, count + 1)]
    rest, holding = total - reach - (count - 1), [1] * (count - 1)
    while rest > 0:
        free = [i for i in range(count - 1) if holding[i] < reach]
        pool, budget = sum([loads[i] for i in free]), rest
        for i in free:
            extra = min(reach - holding[i], max(1, budget * loads[i] // pool), rest)
            holding[i] = holding[i] + extra
            rest = rest - extra
    return np.array([reach] + holding)


def ragged_sizes(key, amount, total, limit, skew):
    if amount == 2:
        one = jax.random.randint(key, (), max(1, total - limit), min(limit, total - 1) + 1)
        return jnp.stack([one, total - one])
    tallies = jnp.asarray(profile(amount, total, limit, skew), jnp.int32)
    couples = (amount - 1) // 2
    donor, sink = tallies[1:1 + 2 * couples:2], tallies[2:2 + 2 * couples:2]
    room = jnp.minimum(donor - 1, limit - sink)
    passed = jax.random.randint(jax.random.fold_in(key, 1), (couples,), 0, 1 << 20) % (room + 1)
    tallies = tallies.at[1:1 + 2 * couples:2].set(donor - passed).at[2:2 + 2 * couples:2].set(sink + passed)
    return tallies[jax.random.permutation(jax.random.fold_in(key, 2), amount)]


def centred(own_key, shape, scale, limit, split=(), kind=jnp.bfloat16):
    drawn = scale * jax.random.normal(own_key, shape, jnp.float32)
    if split:
        drawn = drawn * level_of(own_key, shape, split, -0.22, 0.18)
    return jnp.clip(drawn, -limit, limit).astype(kind)


def setup_inputs(seed: int = 0) -> dict:
    key_list = jax.random.split(jax.random.key(seed), 7)
    query_rows = draw_query_rows(jax.random.fold_in(key_list[6], 71), 0)
    key_rows = draw_key_rows(jax.random.fold_in(key_list[6], 71), 0)
    value_rows = centred(key_list[2], (TOKENS, HEADS * DH), 1.0, 6.0, ((0, 256),))
    forward_out = centred(key_list[3], (TOKENS, HEADS * DH), 1.0, 6.0, ((0, 256),))
    out_grad = centred(key_list[4], (TOKENS, HEADS * DH), 1.0, 6.0, ((0, 256),))
    doc_blocks = ragged_sizes(key_list[5], NDOC, TOKENS // BLOCK, MOST_BLOCKS, 1).astype(jnp.int32)
    return dict(query_rows=query_rows, key_rows=key_rows, value_rows=value_rows, forward_out=forward_out, out_grad=out_grad, doc_blocks=doc_blocks)


def doc_ids(doc_blocks, nblocks):
    ends = jnp.cumsum(doc_blocks).astype(jnp.int32)
    starts = ends - doc_blocks.astype(jnp.int32)
    block_ids = jnp.arange(nblocks, dtype=jnp.int32)
    return (lax.optimization_barrier(jnp.sum((starts[None, :] <= block_ids[:, None]).astype(jnp.int32), axis=1)) - 1).astype(jnp.int32)

def reference(query_rows, key_rows, value_rows, forward_out, out_grad, doc_blocks):
    rows = TOK_DEV
    shards = TOKENS // rows
    features = HEADS * DH
    scale = 1.0 / math.sqrt(DH)
    margin = REACH * rows
    token_docs = jnp.repeat(doc_ids(doc_blocks, TOKENS // BLOCK), BLOCK).astype(jnp.int32)
    padded_docs = jnp.concatenate([jnp.full((margin,), -1, jnp.int32), token_docs])
    padded_keys = jnp.concatenate([jnp.zeros((margin, features), key_rows.dtype), key_rows])
    padded_values = jnp.concatenate([jnp.zeros((margin, features), value_rows.dtype), value_rows])

    def one_shard(carry, shard):
        key_acc, value_acc = carry
        start = (shard * rows).astype(jnp.int32)
        query = lax.dynamic_slice_in_dim(query_rows, start, rows, 0).astype(jnp.float32).reshape(rows, HEADS, DH)
        grads = lax.dynamic_slice_in_dim(out_grad, start, rows, 0).astype(jnp.float32).reshape(rows, HEADS, DH)
        outs = lax.dynamic_slice_in_dim(forward_out, start, rows, 0).astype(jnp.float32).reshape(rows, HEADS, DH)
        keys_win = lax.dynamic_slice_in_dim(padded_keys, start, margin + rows, 0).astype(jnp.float32).reshape(margin + rows, HEADS, DH)
        values_win = lax.dynamic_slice_in_dim(padded_values, start, margin + rows, 0).astype(jnp.float32).reshape(margin + rows, HEADS, DH)
        query_docs = lax.dynamic_slice_in_dim(token_docs, start, rows, 0)
        key_docs = lax.dynamic_slice_in_dim(padded_docs, start, margin + rows, 0)
        query_pos = jnp.arange(rows, dtype=jnp.int32) + margin
        key_pos = jnp.arange(margin + rows, dtype=jnp.int32)
        mask = (query_docs[:, None] == key_docs[None, :]) & (key_pos[None, :] <= query_pos[:, None])
        scores = jnp.einsum('qhd,khd->hqk', query, keys_win) * scale
        masked = jnp.where(mask[None], scores, -1e+30)
        top = lax.optimization_barrier(jnp.max(masked, axis=2))
        logsum = top + jnp.log(lax.optimization_barrier(jnp.sum(jnp.exp(masked - top[..., None]), axis=2)))
        prob = jnp.where(mask[None], jnp.exp(masked - logsum[..., None]), 0.0)
        prob_b = prob.astype(jnp.bfloat16).astype(jnp.float32)
        delta = jnp.einsum('qhd,qhd->hq', grads, outs)
        dprob = jnp.einsum('qhd,khd->hqk', grads, values_win)
        dscore = (prob * (dprob - delta[..., None])).astype(jnp.bfloat16).astype(jnp.float32)
        query_part = jnp.einsum('hqk,khd->qhd', dscore, keys_win) * scale
        key_part = (jnp.einsum('hqk,qhd->khd', dscore, query) * scale).reshape(margin + rows, features)
        value_part = jnp.einsum('hqk,qhd->khd', prob_b, grads).reshape(margin + rows, features)
        old_keys = lax.dynamic_slice_in_dim(key_acc, start, margin + rows, 0)
        old_values = lax.dynamic_slice_in_dim(value_acc, start, margin + rows, 0)
        key_acc = lax.dynamic_update_slice_in_dim(key_acc, old_keys + key_part, start, 0)
        value_acc = lax.dynamic_update_slice_in_dim(value_acc, old_values + value_part, start, 0)
        return ((key_acc, value_acc), query_part.reshape(rows, features).astype(jnp.bfloat16))
    empty = jnp.zeros((margin + TOKENS, features), jnp.float32)
    (key_acc, value_acc), query_parts = lax.scan(one_shard, (empty, empty), jnp.arange(shards, dtype=jnp.int32))
    query_grad = query_parts.reshape(TOKENS, features)
    return (query_grad, key_acc[margin:].astype(jnp.bfloat16), value_acc[margin:].astype(jnp.bfloat16))
```

```python
import math

import jax
import jax.numpy as jnp
from jax import lax
from jax.sharding import PartitionSpec as P

HEADS = 8
DH = 128
BLOCK = 128
REACH = 7
GROUPS = 2


def from_behind(value, axis, steps):
    count = lax.axis_size(axis)
    first, last = (max(0, -steps), min(count, count - steps))
    return lax.ppermute(value, axis, [(source, source + steps) for source in range(first, last)])


def doc_window(doc_blocks, first_block, count):
    ends = jnp.cumsum(doc_blocks)
    starts = ends - doc_blocks
    block_ids = first_block + jnp.arange(count, dtype=jnp.int32)
    found = jnp.sum((starts[None, :] <= block_ids[:, None]).astype(jnp.int32), axis=1) - 1
    return jnp.where(block_ids >= ends[-1], -2, found)


def per_device(query_rows, key_rows, value_rows, forward_out, out_grad, doc_blocks):
    rows, features = query_rows.shape
    scale = 1.0 / math.sqrt(DH)
    axes = ("cx", "cy")
    shard = lax.axis_index(axes)
    per_shard = rows // BLOCK
    window = REACH + 1
    block_docs = doc_window(doc_blocks, shard * per_shard, window * per_shard)
    token_docs = jnp.repeat(block_docs, BLOCK)
    key_docs = token_docs[:rows]
    offsets = jnp.arange(rows, dtype=jnp.int32)

    def allowed(step):
        query_docs = token_docs[step * rows : (step + 1) * rows]
        mask = query_docs[:, None] == key_docs[None, :]
        if step == 0:
            mask = mask & (offsets[None, :] <= offsets[:, None])
        return mask

    masks = [allowed(step) for step in range(window)]

    def to_heads(x):
        return x.reshape(rows, HEADS, DH).transpose(1, 0, 2)

    def from_heads(x):
        return x.transpose(1, 0, 2).reshape(rows, features)

    query_h = to_heads(query_rows)
    grad_h = to_heads(out_grad)
    key_h = to_heads(key_rows)
    value_h = to_heads(value_rows)
    delta = jnp.einsum(
        "hqd,hqd->hq", grad_h, to_heads(forward_out), preferred_element_type=jnp.float32
    )

    def scores_of(q, k, mask):
        s = jnp.einsum("hqd,hkd->hqk", q, k, preferred_element_type=jnp.float32) * scale
        return jnp.where(mask[None], s, -1e30)

    group = HEADS // GROUPS
    query_grads, key_grads, value_grads = [], [], []
    for g in range(GROUPS):
        heads = slice(g * group, (g + 1) * group)
        q_own, do_own, k_own, v_own = query_h[heads], grad_h[heads], key_h[heads], value_h[heads]
        delta_own = delta[heads]

        scores = scores_of(q_own, k_own, masks[0])
        top = jnp.max(scores, axis=2)
        total = jnp.sum(jnp.exp(scores - top[..., None]), axis=2)
        stored = [(q_own, do_own, delta_own)]
        stats = [(top, total)]
        big = jnp.stack([q_own, do_own])
        small = jnp.stack([top, total, delta_own])
        for step in range(1, window):
            big = from_behind(big, axes, -1)
            small = from_behind(small, axes, -1)
            q_in, do_in = big[0], big[1]
            top_in, total_in, delta_in = small[0], small[1], small[2]
            scores = scores_of(q_in, k_own, masks[step])
            part_top = jnp.max(scores, axis=2)
            part_total = jnp.sum(jnp.exp(scores - part_top[..., None]), axis=2)
            merged_top = jnp.maximum(top_in, part_top)
            merged_total = total_in * jnp.exp(top_in - merged_top) + part_total * jnp.exp(
                part_top - merged_top
            )
            stored.append((q_in, do_in, delta_in))
            stats.append((merged_top, merged_total))
            if step < window - 1:
                small = jnp.stack([merged_top, merged_total, delta_in])

        key_acc = None
        value_acc = None
        carry = None
        for stage in range(window):
            step = window - 1 - stage
            q_in, do_in, delta_in = stored[step]
            local_lse = stats[step][0] + jnp.log(stats[step][1])
            if stage == 0:
                lse = local_lse
                dq_in = None
            else:
                carry = from_behind(carry, axes, 1)
                dq_in = carry[:, :rows]
                lse = jnp.where(shard == 0, local_lse, carry[:, rows:].reshape(group, rows))
            mask = masks[step]
            scores = scores_of(q_in, k_own, mask)
            prob = jnp.where(mask[None], jnp.exp(scores - lse[..., None]), 0.0)
            dprob = jnp.einsum("hqd,hkd->hqk", do_in, v_own, preferred_element_type=jnp.float32)
            dscore = (prob * (dprob - delta_in[..., None])).astype(jnp.bfloat16)
            dq_part = jnp.einsum("hqk,hkd->hqd", dscore, k_own, preferred_element_type=jnp.float32)
            key_part = jnp.einsum("hqk,hqd->hkd", dscore, q_in, preferred_element_type=jnp.float32)
            value_part = jnp.einsum(
                "hqk,hqd->hkd", prob.astype(jnp.bfloat16), do_in, preferred_element_type=jnp.float32
            )
            key_acc = key_part if key_acc is None else key_acc + key_part
            value_acc = value_part if value_acc is None else value_acc + value_part
            dq_out = dq_part if dq_in is None else dq_in + dq_part
            if stage < window - 1:
                carry = jnp.concatenate(
                    [dq_out, lse.reshape(group, rows // DH, DH)], axis=1
                )
        query_grads.append(dq_out)
        key_grads.append(key_acc)
        value_grads.append(value_acc)
    query_grad = from_heads(jnp.concatenate(query_grads) * scale).astype(jnp.bfloat16)
    key_grad = from_heads(jnp.concatenate(key_grads) * scale).astype(jnp.bfloat16)
    value_grad = from_heads(jnp.concatenate(value_grads)).astype(jnp.bfloat16)
    return (query_grad, key_grad, value_grad)


def solution(mesh):
    in_specs = (
        P(("cx", "cy"), None),
        P(("cx", "cy"), None),
        P(("cx", "cy"), None),
        P(("cx", "cy"), None),
        P(("cx", "cy"), None),
        P(),
    )
    out_specs = (P(("cx", "cy"), None), P(("cx", "cy"), None), P(("cx", "cy"), None))
    return jax.shard_map(
        per_device, mesh=mesh, in_specs=in_specs, out_specs=out_specs, check_vma=False
    )
```

```python
import math

import jax
import jax.numpy as jnp
from jax import lax
from jax.sharding import PartitionSpec as P

HEADS = 8
DH = 128
BLOCK = 128
REACH = 7
GROUPS = 1


def from_behind(value, axis, steps):
    count = lax.axis_size(axis)
    first, last = (max(0, -steps), min(count, count - steps))
    return lax.ppermute(value, axis, [(source, source + steps) for source in range(first, last)])


def doc_window(doc_blocks, first_block, count):
    ends = jnp.cumsum(doc_blocks)
    starts = ends - doc_blocks
    block_ids = first_block + jnp.arange(count, dtype=jnp.int32)
    found = jnp.sum((starts[None, :] <= block_ids[:, None]).astype(jnp.int32), axis=1) - 1
    return jnp.where(block_ids >= ends[-1], -2, found)


def per_device(query_rows, key_rows, value_rows, forward_out, out_grad, doc_blocks):
    rows, features = query_rows.shape
    scale = 1.0 / math.sqrt(DH)
    axes = ("cx", "cy")
    shard = lax.axis_index(axes)
    per_shard = rows // BLOCK
    window = REACH + 1
    block_docs = doc_window(doc_blocks, shard * per_shard, window * per_shard)
    token_docs = jnp.repeat(block_docs, BLOCK)
    key_docs = token_docs[:rows]
    offsets = jnp.arange(rows, dtype=jnp.int32)

    def allowed(step):
        query_docs = token_docs[step * rows : (step + 1) * rows]
        mask = query_docs[:, None] == key_docs[None, :]
        if step == 0:
            mask = mask & (offsets[None, :] <= offsets[:, None])
        return mask

    masks = [allowed(step) for step in range(window)]

    def to_heads(x):
        return x.reshape(rows, HEADS, DH).transpose(1, 0, 2)

    def from_heads(x):
        return x.transpose(1, 0, 2).reshape(rows, features)

    query_h = to_heads(query_rows)
    grad_h = to_heads(out_grad)
    key_h = to_heads(key_rows)
    value_h = to_heads(value_rows)
    delta = jnp.einsum(
        "hqd,hqd->hq", grad_h, to_heads(forward_out), preferred_element_type=jnp.float32
    )

    def scores_of(q, k, mask):
        s = jnp.einsum("hqd,hkd->hqk", q, k, preferred_element_type=jnp.float32) * scale
        return jnp.where(mask[None], s, -1e30)

    group = HEADS // GROUPS
    query_grads, key_grads, value_grads = [], [], []
    for g in range(GROUPS):
        heads = slice(g * group, (g + 1) * group)
        q_own, do_own, k_own, v_own = query_h[heads], grad_h[heads], key_h[heads], value_h[heads]
        delta_own = delta[heads]

        scores = scores_of(q_own, k_own, masks[0])
        top = jnp.max(scores, axis=2)
        total = jnp.sum(jnp.exp(scores - top[..., None]), axis=2)
        stored = [(q_own, do_own, delta_own)]
        stats = [(top, total)]
        big = jnp.stack([q_own, do_own])
        small = jnp.concatenate([top, total, delta_own], axis=1)
        for step in range(1, window):
            big = from_behind(big, axes, -1)
            small = from_behind(small, axes, -1)
            q_in, do_in = big[0], big[1]
            top_in, total_in, delta_in = small[:, :rows], small[:, rows : 2 * rows], small[:, 2 * rows :]
            scores = scores_of(q_in, k_own, masks[step])
            part_top = jnp.max(scores, axis=2)
            part_total = jnp.sum(jnp.exp(scores - part_top[..., None]), axis=2)
            merged_top = jnp.maximum(top_in, part_top)
            merged_total = total_in * jnp.exp(top_in - merged_top) + part_total * jnp.exp(
                part_top - merged_top
            )
            stored.append((q_in, do_in, delta_in))
            stats.append((merged_top, merged_total))
            if step < window - 1:
                small = jnp.concatenate([merged_top, merged_total, delta_in], axis=1)

        key_acc = None
        value_acc = None
        carry = None
        for stage in range(window):
            step = window - 1 - stage
            q_in, do_in, delta_in = stored[step]
            local_lse = stats[step][0] + jnp.log(stats[step][1])
            if stage == 0:
                lse = local_lse
                dq_in = None
            else:
                dq_in, lse_in = from_behind(carry, axes, 1)
                lse = jnp.where(shard == 0, local_lse, lse_in)
            mask = masks[step]
            scores = scores_of(q_in, k_own, mask)
            prob = jnp.where(mask[None], jnp.exp(scores - lse[..., None]), 0.0)
            dprob = jnp.einsum("hqd,hkd->hqk", do_in, v_own, preferred_element_type=jnp.float32)
            dscore = (prob * (dprob - delta_in[..., None])).astype(jnp.bfloat16)
            dq_part = jnp.einsum("hqk,hkd->hqd", dscore, k_own, preferred_element_type=jnp.float32)
            key_part = jnp.einsum("hqk,hqd->hkd", dscore, q_in, preferred_element_type=jnp.float32)
            value_part = jnp.einsum(
                "hqk,hqd->hkd", prob.astype(jnp.bfloat16), do_in, preferred_element_type=jnp.float32
            )
            key_acc = key_part if key_acc is None else key_acc + key_part
            value_acc = value_part if value_acc is None else value_acc + value_part
            dq_out = dq_part if dq_in is None else dq_in + dq_part
            if stage < window - 1:
                carry = (dq_out, lse)
        query_grads.append(dq_out)
        key_grads.append(key_acc)
        value_grads.append(value_acc)
    query_grad = from_heads(jnp.concatenate(query_grads) * scale).astype(jnp.bfloat16)
    key_grad = from_heads(jnp.concatenate(key_grads) * scale).astype(jnp.bfloat16)
    value_grad = from_heads(jnp.concatenate(value_grads)).astype(jnp.bfloat16)
    return (query_grad, key_grad, value_grad)


def solution(mesh):
    in_specs = (
        P(("cx", "cy"), None),
        P(("cx", "cy"), None),
        P(("cx", "cy"), None),
        P(("cx", "cy"), None),
        P(("cx", "cy"), None),
        P(),
    )
    out_specs = (P(("cx", "cy"), None), P(("cx", "cy"), None), P(("cx", "cy"), None))
    return jax.shard_map(
        per_device, mesh=mesh, in_specs=in_specs, out_specs=out_specs, check_vma=False
    )
```

```python
import math

import jax
import jax.numpy as jnp
from jax import lax
from jax.sharding import PartitionSpec as P

HEADS = 8
DH = 128
BLOCK = 128
REACH = 7
GROUPS = 1


def from_behind(value, axis, steps):
    count = lax.axis_size(axis)
    first, last = (max(0, -steps), min(count, count - steps))
    return lax.ppermute(value, axis, [(source, source + steps) for source in range(first, last)])


def doc_window(doc_blocks, first_block, count):
    ends = jnp.cumsum(doc_blocks)
    starts = ends - doc_blocks
    block_ids = first_block + jnp.arange(count, dtype=jnp.int32)
    found = jnp.sum((starts[None, :] <= block_ids[:, None]).astype(jnp.int32), axis=1) - 1
    return jnp.where(block_ids >= ends[-1], -2, found)


def per_device(query_rows, key_rows, value_rows, forward_out, out_grad, doc_blocks):
    rows, features = query_rows.shape
    scale = 1.0 / math.sqrt(DH)
    axes = ("cx", "cy")
    shard = lax.axis_index(axes)
    per_shard = rows // BLOCK
    window = REACH + 1
    block_docs = doc_window(doc_blocks, shard * per_shard, window * per_shard)
    token_docs = jnp.repeat(block_docs, BLOCK)
    key_docs = token_docs[:rows]
    offsets = jnp.arange(rows, dtype=jnp.int32)

    def allowed(step):
        query_docs = token_docs[step * rows : (step + 1) * rows]
        mask = query_docs[:, None] == key_docs[None, :]
        if step == 0:
            mask = mask & (offsets[None, :] <= offsets[:, None])
        return mask

    masks = [allowed(step) for step in range(window)]

    def to_heads(x):
        return x.reshape(rows, HEADS, DH).transpose(1, 0, 2)

    def from_heads(x):
        return x.transpose(1, 0, 2).reshape(rows, features)

    query_h = to_heads(query_rows)
    grad_h = to_heads(out_grad)
    key_h = to_heads(key_rows)
    value_h = to_heads(value_rows)
    delta = jnp.einsum(
        "hqd,hqd->hq", grad_h, to_heads(forward_out), preferred_element_type=jnp.float32
    )

    def scores_of(q, k, mask):
        s = jnp.einsum("hqd,hkd->hqk", q, k, preferred_element_type=jnp.float32) * scale
        return jnp.where(mask[None], s, -1e30)

    group = HEADS // GROUPS
    query_grads, key_grads, value_grads = [], [], []
    for g in range(GROUPS):
        heads = slice(g * group, (g + 1) * group)
        q_own, do_own, k_own, v_own = query_h[heads], grad_h[heads], key_h[heads], value_h[heads]
        delta_own = delta[heads]

        scores = scores_of(q_own, k_own, masks[0])
        top = jnp.max(scores, axis=2)
        total = jnp.sum(jnp.exp(scores - top[..., None]), axis=2)
        stored = [(q_own, do_own, delta_own)]
        stats = [(top, total)]
        big = (q_own, do_own)
        small = jnp.concatenate([top, total, delta_own], axis=1)
        for step in range(1, window):
            big = from_behind(big, axes, -1)
            small = from_behind(small, axes, -1)
            q_in, do_in = big
            top_in, total_in, delta_in = small[:, :rows], small[:, rows : 2 * rows], small[:, 2 * rows :]
            scores = scores_of(q_in, k_own, masks[step])
            part_top = jnp.max(scores, axis=2)
            part_total = jnp.sum(jnp.exp(scores - part_top[..., None]), axis=2)
            merged_top = jnp.maximum(top_in, part_top)
            merged_total = total_in * jnp.exp(top_in - merged_top) + part_total * jnp.exp(
                part_top - merged_top
            )
            stored.append((q_in, do_in, delta_in))
            stats.append((merged_top, merged_total))
            if step < window - 1:
                small = jnp.concatenate([merged_top, merged_total, delta_in], axis=1)

        key_acc = None
        value_acc = None
        carry = None
        for stage in range(window):
            step = window - 1 - stage
            q_in, do_in, delta_in = stored[step]
            local_lse = stats[step][0] + jnp.log(stats[step][1])
            if stage == 0:
                lse = local_lse
                dq_in = None
            else:
                dq_low, dq_high, lse_in = from_behind(carry, axes, 1)
                dq_in = jnp.concatenate([dq_low, dq_high])
                lse = jnp.where(shard == 0, local_lse, lse_in)
            mask = masks[step]
            scores = scores_of(q_in, k_own, mask)
            prob = jnp.where(mask[None], jnp.exp(scores - lse[..., None]), 0.0)
            dprob = jnp.einsum("hqd,hkd->hqk", do_in, v_own, preferred_element_type=jnp.float32)
            dscore = (prob * (dprob - delta_in[..., None])).astype(jnp.bfloat16)
            dq_part = jnp.einsum("hqk,hkd->hqd", dscore, k_own, preferred_element_type=jnp.float32)
            key_part = jnp.einsum("hqk,hqd->hkd", dscore, q_in, preferred_element_type=jnp.float32)
            value_part = jnp.einsum(
                "hqk,hqd->hkd", prob.astype(jnp.bfloat16), do_in, preferred_element_type=jnp.float32
            )
            key_acc = key_part if key_acc is None else key_acc + key_part
            value_acc = value_part if value_acc is None else value_acc + value_part
            dq_out = dq_part if dq_in is None else dq_in + dq_part
            if stage < window - 1:
                carry = (dq_out[: group // 2], dq_out[group // 2 :], lse)
        query_grads.append(dq_out)
        key_grads.append(key_acc)
        value_grads.append(value_acc)
    query_grad = from_heads(jnp.concatenate(query_grads) * scale).astype(jnp.bfloat16)
    key_grad = from_heads(jnp.concatenate(key_grads) * scale).astype(jnp.bfloat16)
    value_grad = from_heads(jnp.concatenate(value_grads)).astype(jnp.bfloat16)
    return (query_grad, key_grad, value_grad)


def solution(mesh):
    in_specs = (
        P(("cx", "cy"), None),
        P(("cx", "cy"), None),
        P(("cx", "cy"), None),
        P(("cx", "cy"), None),
        P(("cx", "cy"), None),
        P(),
    )
    out_specs = (P(("cx", "cy"), None), P(("cx", "cy"), None), P(("cx", "cy"), None))
    return jax.shard_map(
        per_device, mesh=mesh, in_specs=in_specs, out_specs=out_specs, check_vma=False
    )
```

```python
import math

import jax
import jax.numpy as jnp
from jax import lax
from jax.sharding import PartitionSpec as P

HEADS = 8
DH = 128
BLOCK = 128
REACH = 7


def from_behind(value, axis, steps):
    count = lax.axis_size(axis)
    first, last = (max(0, -steps), min(count, count - steps))
    return lax.ppermute(value, axis, [(source, source + steps) for source in range(first, last)])


def doc_window(doc_blocks, first_block, count):
    ends = jnp.cumsum(doc_blocks)
    starts = ends - doc_blocks
    block_ids = first_block + jnp.arange(count, dtype=jnp.int32)
    found = jnp.sum((starts[None, :] <= block_ids[:, None]).astype(jnp.int32), axis=1) - 1
    return jnp.where(block_ids >= ends[-1], -2, found)


def per_device(query_rows, key_rows, value_rows, forward_out, out_grad, doc_blocks):
    rows, features = query_rows.shape
    scale = 1.0 / math.sqrt(DH)
    axes = ("cx", "cy")
    shard = lax.axis_index(axes)
    per_shard = rows // BLOCK
    window = REACH + 1
    block_docs = doc_window(doc_blocks, (shard - REACH) * per_shard, (2 * REACH + 1) * per_shard)
    token_docs = jnp.repeat(block_docs, BLOCK)

    def docs_at(step):
        return token_docs[(REACH + step) * rows : (REACH + step + 1) * rows]

    local_docs = docs_at(0)
    offsets = jnp.arange(rows, dtype=jnp.int32)
    causal = offsets[None, :] <= offsets[:, None]
    query_masks = [local_docs[:, None] == docs_at(-step)[None, :] for step in range(window)]
    query_masks[0] = query_masks[0] & causal
    key_masks = [docs_at(step)[:, None] == local_docs[None, :] for step in range(window)]

    def to_heads(x):
        return x.reshape(rows, HEADS, DH).transpose(1, 0, 2)

    def from_heads(x):
        return x.transpose(1, 0, 2).reshape(rows, features)

    query_h = to_heads(query_rows)
    grad_h = to_heads(out_grad)
    key_h = to_heads(key_rows)
    value_h = to_heads(value_rows)
    delta = jnp.einsum(
        "hqd,hqd->hq", grad_h, to_heads(forward_out), preferred_element_type=jnp.float32
    )

    key_values = [(key_h, value_h)]
    query_grads = [(query_h, grad_h)]
    moving_kv = (key_h, value_h)
    moving_qg = (query_h, grad_h)
    for step in range(1, window):
        moving_kv = from_behind(moving_kv, axes, 1)
        moving_qg = from_behind(moving_qg, axes, -1)
        key_values.append(moving_kv)
        query_grads.append(moving_qg)

    def scores_of(q, k, mask):
        s = jnp.einsum("hqd,hkd->hqk", q, k, preferred_element_type=jnp.float32) * scale
        return jnp.where(mask[None], s, -1e30)

    def tile_stats(q, k, mask):
        s = scores_of(q, k, mask)
        top = jnp.max(s, axis=2)
        return (top, jnp.sum(jnp.exp(s - top[..., None]), axis=2))

    stats = tile_stats(query_h, key_h, query_masks[0])
    for step in range(1, window):
        part = tile_stats(query_h, key_values[step][0], query_masks[step])
        top = jnp.maximum(stats[0], part[0])
        total = stats[1] * jnp.exp(stats[0] - top) + part[1] * jnp.exp(part[0] - top)
        stats = (top, total)
    logsum = stats[0] + jnp.log(stats[1])

    row_stats = jnp.concatenate([logsum, delta], axis=1)
    later_stats = [row_stats] + [from_behind(row_stats, axes, -step) for step in range(1, window)]

    def tile_grads(q, g, k, v, lse, dlt, mask):
        s = scores_of(q, k, mask)
        prob = jnp.where(mask[None], jnp.exp(s - lse[..., None]), 0.0)
        dprob = jnp.einsum("hqd,hkd->hqk", g, v, preferred_element_type=jnp.float32)
        dscore = (prob * (dprob - dlt[..., None])).astype(jnp.bfloat16)
        return prob.astype(jnp.bfloat16), dscore

    prob_b, dscore = tile_grads(query_h, grad_h, key_h, value_h, logsum, delta, query_masks[0])
    query_acc = jnp.einsum("hqk,hkd->hqd", dscore, key_h, preferred_element_type=jnp.float32)
    key_acc = jnp.einsum("hqk,hqd->hkd", dscore, query_h, preferred_element_type=jnp.float32)
    value_acc = jnp.einsum("hqk,hqd->hkd", prob_b, grad_h, preferred_element_type=jnp.float32)
    for step in range(1, window):
        k_in, v_in = key_values[step]
        _, dscore = tile_grads(query_h, grad_h, k_in, v_in, logsum, delta, query_masks[step])
        query_acc = query_acc + jnp.einsum(
            "hqk,hkd->hqd", dscore, k_in, preferred_element_type=jnp.float32
        )
        q_in, g_in = query_grads[step]
        lse_in = later_stats[step][:, :rows]
        delta_in = later_stats[step][:, rows:]
        prob_b, dscore = tile_grads(q_in, g_in, key_h, value_h, lse_in, delta_in, key_masks[step])
        key_acc = key_acc + jnp.einsum(
            "hqk,hqd->hkd", dscore, q_in, preferred_element_type=jnp.float32
        )
        value_acc = value_acc + jnp.einsum(
            "hqk,hqd->hkd", prob_b, g_in, preferred_element_type=jnp.float32
        )
    query_grad = from_heads(query_acc * scale).astype(jnp.bfloat16)
    key_grad = from_heads(key_acc * scale).astype(jnp.bfloat16)
    value_grad = from_heads(value_acc).astype(jnp.bfloat16)
    return (query_grad, key_grad, value_grad)


def solution(mesh):
    in_specs = (
        P(("cx", "cy"), None),
        P(("cx", "cy"), None),
        P(("cx", "cy"), None),
        P(("cx", "cy"), None),
        P(("cx", "cy"), None),
        P(),
    )
    out_specs = (P(("cx", "cy"), None), P(("cx", "cy"), None), P(("cx", "cy"), None))
    return jax.shard_map(
        per_device, mesh=mesh, in_specs=in_specs, out_specs=out_specs, check_vma=False
    )
```

```python
import math

import jax
import jax.numpy as jnp
from jax import lax
from jax.sharding import PartitionSpec as P

HEADS = 8
DH = 128
BLOCK = 128
REACH = 7


def from_behind(value, axis, steps):
    count = lax.axis_size(axis)
    first, last = (max(0, -steps), min(count, count - steps))
    return lax.ppermute(value, axis, [(source, source + steps) for source in range(first, last)])


def doc_window(doc_blocks, first_block, count):
    ends = jnp.cumsum(doc_blocks)
    starts = ends - doc_blocks
    block_ids = first_block + jnp.arange(count, dtype=jnp.int32)
    found = jnp.sum((starts[None, :] <= block_ids[:, None]).astype(jnp.int32), axis=1) - 1
    return jnp.where(block_ids >= ends[-1], -2, found)


def per_device(query_rows, key_rows, value_rows, forward_out, out_grad, doc_blocks):
    rows, features = query_rows.shape
    scale = 1.0 / math.sqrt(DH)
    axes = ("cx", "cy")
    shard = lax.axis_index(axes)
    per_shard = rows // BLOCK
    window = REACH + 1
    block_docs = doc_window(doc_blocks, (shard - REACH) * per_shard, (2 * REACH + 1) * per_shard)
    token_docs = jnp.repeat(block_docs, BLOCK)

    def docs_at(step):
        return token_docs[(REACH + step) * rows : (REACH + step + 1) * rows]

    local_docs = docs_at(0)
    offsets = jnp.arange(rows, dtype=jnp.int32)
    causal = offsets[None, :] <= offsets[:, None]
    query_masks = [local_docs[:, None] == docs_at(-step)[None, :] for step in range(window)]
    query_masks[0] = query_masks[0] & causal
    key_masks = [docs_at(step)[:, None] == local_docs[None, :] for step in range(window)]

    def to_heads(x):
        return x.reshape(rows, HEADS, DH).transpose(1, 0, 2)

    def from_heads(x):
        return x.transpose(1, 0, 2).reshape(rows, features)

    query_h = to_heads(query_rows)
    grad_h = to_heads(out_grad)
    key_h = to_heads(key_rows)
    value_h = to_heads(value_rows)
    delta = jnp.einsum(
        "hqd,hqd->hq", grad_h, to_heads(forward_out), preferred_element_type=jnp.float32
    )

    key_values = [(key_h, value_h)]
    query_grads = [(query_h, grad_h)]
    moving_kv = (key_h, value_h)
    moving_qg = (query_h, grad_h)
    for step in range(1, window):
        moving_kv = from_behind(moving_kv, axes, 1)
        moving_qg = from_behind(moving_qg, axes, -1)
        key_values.append(moving_kv)
        query_grads.append(moving_qg)

    def scores_of(q, k, mask):
        s = jnp.einsum("hqd,hkd->hqk", q, k, preferred_element_type=jnp.float32) * scale
        return jnp.where(mask[None], s, -1e30)

    def tile_stats(q, k, mask):
        s = scores_of(q, k, mask)
        top = jnp.max(s, axis=2)
        return (top, jnp.sum(jnp.exp(s - top[..., None]), axis=2))

    query_live = [local_docs[0] == docs_at(-step)[rows - 1] for step in range(window)]
    key_live = [docs_at(step)[0] == local_docs[rows - 1] for step in range(window)]

    def merged(step, stats):
        part = tile_stats(query_h, key_values[step][0], query_masks[step])
        top = jnp.maximum(stats[0], part[0])
        total = stats[1] * jnp.exp(stats[0] - top) + part[1] * jnp.exp(part[0] - top)
        return (top, total)

    stats = tile_stats(query_h, key_h, query_masks[0])
    for step in range(1, window):
        stats = lax.cond(
            query_live[step], lambda st, step=step: merged(step, st), lambda st: st, stats
        )
    logsum = stats[0] + jnp.log(stats[1])

    row_stats = jnp.concatenate([logsum, delta], axis=1)
    later_stats = [row_stats] + [from_behind(row_stats, axes, -step) for step in range(1, window)]

    def tile_grads(q, g, k, v, lse, dlt, mask):
        s = scores_of(q, k, mask)
        prob = jnp.where(mask[None], jnp.exp(s - lse[..., None]), 0.0)
        dprob = jnp.einsum("hqd,hkd->hqk", g, v, preferred_element_type=jnp.float32)
        dscore = (prob * (dprob - dlt[..., None])).astype(jnp.bfloat16)
        return prob.astype(jnp.bfloat16), dscore

    prob_b, dscore = tile_grads(query_h, grad_h, key_h, value_h, logsum, delta, query_masks[0])
    query_acc = jnp.einsum("hqk,hkd->hqd", dscore, key_h, preferred_element_type=jnp.float32)
    key_acc = jnp.einsum("hqk,hqd->hkd", dscore, query_h, preferred_element_type=jnp.float32)
    value_acc = jnp.einsum("hqk,hqd->hkd", prob_b, grad_h, preferred_element_type=jnp.float32)
    def query_tile(step, acc):
        k_in, v_in = key_values[step]
        _, dscore = tile_grads(query_h, grad_h, k_in, v_in, logsum, delta, query_masks[step])
        return acc + jnp.einsum("hqk,hkd->hqd", dscore, k_in, preferred_element_type=jnp.float32)

    def key_tile(step, accs):
        q_in, g_in = query_grads[step]
        lse_in = later_stats[step][:, :rows]
        delta_in = later_stats[step][:, rows:]
        prob_b, dscore = tile_grads(q_in, g_in, key_h, value_h, lse_in, delta_in, key_masks[step])
        k_part = jnp.einsum("hqk,hqd->hkd", dscore, q_in, preferred_element_type=jnp.float32)
        v_part = jnp.einsum("hqk,hqd->hkd", prob_b, g_in, preferred_element_type=jnp.float32)
        return (accs[0] + k_part, accs[1] + v_part)

    for step in range(1, window):
        query_acc = lax.cond(
            query_live[step], lambda a, step=step: query_tile(step, a), lambda a: a, query_acc
        )
    for step in range(1, window):
        key_acc, value_acc = lax.cond(
            key_live[step],
            lambda a, step=step: key_tile(step, a),
            lambda a: a,
            (key_acc, value_acc),
        )
    query_grad = from_heads(query_acc * scale).astype(jnp.bfloat16)
    key_grad = from_heads(key_acc * scale).astype(jnp.bfloat16)
    value_grad = from_heads(value_acc).astype(jnp.bfloat16)
    return (query_grad, key_grad, value_grad)


def solution(mesh):
    in_specs = (
        P(("cx", "cy"), None),
        P(("cx", "cy"), None),
        P(("cx", "cy"), None),
        P(("cx", "cy"), None),
        P(("cx", "cy"), None),
        P(),
    )
    out_specs = (P(("cx", "cy"), None), P(("cx", "cy"), None), P(("cx", "cy"), None))
    return jax.shard_map(
        per_device, mesh=mesh, in_specs=in_specs, out_specs=out_specs, check_vma=False
    )
```

```python
import math

import jax
import jax.numpy as jnp
from jax import lax
from jax.sharding import PartitionSpec as P

HEADS = 8
DH = 128
BLOCK = 128
REACH = 7


def from_behind(value, axis, steps):
    count = lax.axis_size(axis)
    first, last = (max(0, -steps), min(count, count - steps))
    return lax.ppermute(value, axis, [(source, source + steps) for source in range(first, last)])


def doc_window(doc_blocks, first_block, count):
    ends = jnp.cumsum(doc_blocks)
    starts = ends - doc_blocks
    block_ids = first_block + jnp.arange(count, dtype=jnp.int32)
    found = jnp.sum((starts[None, :] <= block_ids[:, None]).astype(jnp.int32), axis=1) - 1
    return jnp.where(block_ids >= ends[-1], -2, found)


def per_device(query_rows, key_rows, value_rows, forward_out, out_grad, doc_blocks):
    rows, features = query_rows.shape
    scale = 1.0 / math.sqrt(DH)
    axes = ("cx", "cy")
    shard = lax.axis_index(axes)
    per_shard = rows // BLOCK
    window = REACH + 1
    block_docs = doc_window(doc_blocks, (shard - REACH) * per_shard, (2 * REACH + 1) * per_shard)
    token_docs = jnp.repeat(block_docs, BLOCK)

    def docs_at(step):
        return token_docs[(REACH + step) * rows : (REACH + step + 1) * rows]

    local_docs = docs_at(0)
    offsets = jnp.arange(rows, dtype=jnp.int32)
    causal = offsets[None, :] <= offsets[:, None]
    query_masks = [local_docs[:, None] == docs_at(-step)[None, :] for step in range(window)]
    query_masks[0] = query_masks[0] & causal
    key_masks = [local_docs[:, None] == docs_at(step)[None, :] for step in range(window)]

    def to_heads(x):
        return x.reshape(rows, HEADS, DH).transpose(1, 0, 2)

    def from_heads(x):
        return x.transpose(1, 0, 2).reshape(rows, features)

    query_h = to_heads(query_rows)
    grad_h = to_heads(out_grad)
    key_h = to_heads(key_rows)
    value_h = to_heads(value_rows)
    delta = jnp.einsum(
        "hqd,hqd->hq", grad_h, to_heads(forward_out), preferred_element_type=jnp.float32
    )

    key_values = [(key_h, value_h)]
    query_grads = [(query_h, grad_h)]
    moving_kv = (key_h, value_h)
    moving_qg = (query_h, grad_h)
    for step in range(1, window):
        moving_kv = from_behind(moving_kv, axes, 1)
        moving_qg = from_behind(moving_qg, axes, -1)
        key_values.append(moving_kv)
        query_grads.append(moving_qg)

    def scores_of(q, k, mask):
        s = jnp.einsum("hqd,hkd->hqk", q, k, preferred_element_type=jnp.float32) * scale
        return jnp.where(mask[None], s, -1e30)

    def tile_stats(q, k, mask):
        s = scores_of(q, k, mask)
        top = jnp.max(s, axis=2)
        return (top, jnp.sum(jnp.exp(s - top[..., None]), axis=2))

    query_live = [local_docs[0] == docs_at(-step)[rows - 1] for step in range(window)]
    key_live = [docs_at(step)[0] == local_docs[rows - 1] for step in range(window)]

    def merged(step, stats):
        part = tile_stats(query_h, key_values[step][0], query_masks[step])
        top = jnp.maximum(stats[0], part[0])
        total = stats[1] * jnp.exp(stats[0] - top) + part[1] * jnp.exp(part[0] - top)
        return (top, total)

    stats = tile_stats(query_h, key_h, query_masks[0])
    for step in range(1, window):
        stats = lax.cond(
            query_live[step], lambda st, step=step: merged(step, st), lambda st: st, stats
        )
    logsum = stats[0] + jnp.log(stats[1])

    row_stats = jnp.concatenate([logsum, delta], axis=1)
    gathered = lax.all_gather(row_stats, "cy")
    following = from_behind(gathered, "cx", -1)
    both = jnp.concatenate([gathered, following])
    later = lax.dynamic_slice_in_dim(both, lax.axis_index("cy") + 1, REACH, 0)
    later_stats = [row_stats] + [later[step - 1] for step in range(1, window)]

    def tile_grads(q, g, k, v, lse, dlt, mask):
        s = scores_of(q, k, mask)
        prob = jnp.where(mask[None], jnp.exp(s - lse[..., None]), 0.0)
        dprob = jnp.einsum("hqd,hkd->hqk", g, v, preferred_element_type=jnp.float32)
        dscore = (prob * (dprob - dlt[..., None])).astype(jnp.bfloat16)
        return prob.astype(jnp.bfloat16), dscore

    prob_b, dscore = tile_grads(query_h, grad_h, key_h, value_h, logsum, delta, query_masks[0])
    query_acc = jnp.einsum("hqk,hkd->hqd", dscore, key_h, preferred_element_type=jnp.float32)
    key_acc = jnp.einsum("hqk,hqd->hkd", dscore, query_h, preferred_element_type=jnp.float32)
    value_acc = jnp.einsum("hqk,hqd->hkd", prob_b, grad_h, preferred_element_type=jnp.float32)
    def query_tile(step, acc):
        k_in, v_in = key_values[step]
        _, dscore = tile_grads(query_h, grad_h, k_in, v_in, logsum, delta, query_masks[step])
        return acc + jnp.einsum("hqk,hkd->hqd", dscore, k_in, preferred_element_type=jnp.float32)

    def key_tile(step, accs):
        q_in, g_in = query_grads[step]
        lse_in = later_stats[step][:, :rows]
        delta_in = later_stats[step][:, rows:]
        mask = key_masks[step]
        s = jnp.einsum("hkd,hqd->hkq", key_h, q_in, preferred_element_type=jnp.float32) * scale
        s = jnp.where(mask[None], s, -1e30)
        prob = jnp.where(mask[None], jnp.exp(s - lse_in[:, None, :]), 0.0)
        dprob = jnp.einsum("hkd,hqd->hkq", value_h, g_in, preferred_element_type=jnp.float32)
        dscore = (prob * (dprob - delta_in[:, None, :])).astype(jnp.bfloat16)
        k_part = jnp.einsum("hkq,hqd->hkd", dscore, q_in, preferred_element_type=jnp.float32)
        v_part = jnp.einsum(
            "hkq,hqd->hkd", prob.astype(jnp.bfloat16), g_in, preferred_element_type=jnp.float32
        )
        return (accs[0] + k_part, accs[1] + v_part)

    for step in range(1, window):
        query_acc = lax.cond(
            query_live[step], lambda a, step=step: query_tile(step, a), lambda a: a, query_acc
        )
    for step in range(1, window):
        key_acc, value_acc = lax.cond(
            key_live[step],
            lambda a, step=step: key_tile(step, a),
            lambda a: a,
            (key_acc, value_acc),
        )
    query_grad = from_heads(query_acc * scale).astype(jnp.bfloat16)
    key_grad = from_heads(key_acc * scale).astype(jnp.bfloat16)
    value_grad = from_heads(value_acc).astype(jnp.bfloat16)
    return (query_grad, key_grad, value_grad)


def solution(mesh):
    in_specs = (
        P(("cx", "cy"), None),
        P(("cx", "cy"), None),
        P(("cx", "cy"), None),
        P(("cx", "cy"), None),
        P(("cx", "cy"), None),
        P(),
    )
    out_specs = (P(("cx", "cy"), None), P(("cx", "cy"), None), P(("cx", "cy"), None))
    return jax.shard_map(
        per_device, mesh=mesh, in_specs=in_specs, out_specs=out_specs, check_vma=False
    )
```

```python
import math

import jax
import jax.numpy as jnp
from jax import lax
from jax.sharding import PartitionSpec as P

HEADS = 8
DH = 128
BLOCK = 128
REACH = 7


def from_behind(value, axis, steps):
    count = lax.axis_size(axis)
    first, last = (max(0, -steps), min(count, count - steps))
    return lax.ppermute(value, axis, [(source, source + steps) for source in range(first, last)])


def doc_window(doc_blocks, first_block, count):
    ends = jnp.cumsum(doc_blocks)
    starts = ends - doc_blocks
    block_ids = first_block + jnp.arange(count, dtype=jnp.int32)
    found = jnp.sum((starts[None, :] <= block_ids[:, None]).astype(jnp.int32), axis=1) - 1
    return jnp.where(block_ids >= ends[-1], -2, found)


def per_device(query_rows, key_rows, value_rows, forward_out, out_grad, doc_blocks):
    rows, features = query_rows.shape
    scale = 1.0 / math.sqrt(DH)
    axes = ("cx", "cy")
    shard = lax.axis_index(axes)
    per_shard = rows // BLOCK
    window = REACH + 1
    block_docs = doc_window(doc_blocks, (shard - REACH) * per_shard, (2 * REACH + 1) * per_shard)
    token_docs = jnp.repeat(block_docs, BLOCK)

    def docs_at(step):
        return token_docs[(REACH + step) * rows : (REACH + step + 1) * rows]

    local_docs = docs_at(0)
    offsets = jnp.arange(rows, dtype=jnp.int32)
    causal = offsets[None, :] <= offsets[:, None]
    query_masks = [local_docs[:, None] == docs_at(-step)[None, :] for step in range(window)]
    query_masks[0] = query_masks[0] & causal
    key_masks = [local_docs[:, None] == docs_at(step)[None, :] for step in range(window)]

    def to_heads(x):
        return x.reshape(rows, HEADS, DH).transpose(1, 0, 2)

    def from_heads(x):
        return x.transpose(1, 0, 2).reshape(rows, features)

    query_h = to_heads(query_rows)
    grad_h = to_heads(out_grad)
    key_h = to_heads(key_rows)
    value_h = to_heads(value_rows)
    delta = jnp.einsum(
        "hqd,hqd->hq", grad_h, to_heads(forward_out), preferred_element_type=jnp.float32
    )

    key_values = [(key_h, value_h)]
    query_grads = [(query_h, grad_h)]
    moving_kv = (key_h, value_h)
    moving_qg = (query_h, grad_h)
    for step in range(1, window):
        moving_kv = from_behind(moving_kv, axes, 1)
        moving_qg = from_behind(moving_qg, axes, -1)
        key_values.append(moving_kv)
        query_grads.append(moving_qg)

    def scores_of(q, k, mask):
        s = jnp.einsum("hqd,hkd->hqk", q, k, preferred_element_type=jnp.float32) * scale
        return jnp.where(mask[None], s, -1e30)

    def tile_stats(q, k, mask):
        s = scores_of(q, k, mask)
        top = jnp.max(s, axis=2)
        return (top, jnp.sum(jnp.exp(s - top[..., None]), axis=2))

    def merged(step, stats):
        part = tile_stats(query_h, key_values[step][0], query_masks[step])
        top = jnp.maximum(stats[0], part[0])
        total = stats[1] * jnp.exp(stats[0] - top) + part[1] * jnp.exp(part[0] - top)
        return (top, total)

    stats = tile_stats(query_h, key_h, query_masks[0])
    for step in range(1, window):
        stats = merged(step, stats)
    logsum = stats[0] + jnp.log(stats[1])

    row_stats = jnp.concatenate([logsum, delta], axis=1)
    later_stats = [row_stats] + [from_behind(row_stats, axes, -step) for step in range(1, window)]

    def tile_grads(q, g, k, v, lse, dlt, mask):
        s = scores_of(q, k, mask)
        prob = jnp.where(mask[None], jnp.exp(s - lse[..., None]), 0.0)
        dprob = jnp.einsum("hqd,hkd->hqk", g, v, preferred_element_type=jnp.float32)
        dscore = (prob * (dprob - dlt[..., None])).astype(jnp.bfloat16)
        return prob.astype(jnp.bfloat16), dscore

    prob_b, dscore = lax.optimization_barrier(
        tile_grads(query_h, grad_h, key_h, value_h, logsum, delta, query_masks[0])
    )
    query_acc = jnp.einsum("hqk,hkd->hqd", dscore, key_h, preferred_element_type=jnp.float32)
    key_acc = jnp.einsum("hqk,hqd->hkd", dscore, query_h, preferred_element_type=jnp.float32)
    value_acc = jnp.einsum("hqk,hqd->hkd", prob_b, grad_h, preferred_element_type=jnp.float32)

    def query_tile(step, acc):
        k_in, v_in = key_values[step]
        dscore = lax.optimization_barrier(
            tile_grads(query_h, grad_h, k_in, v_in, logsum, delta, query_masks[step])[1]
        )
        return acc + jnp.einsum("hqk,hkd->hqd", dscore, k_in, preferred_element_type=jnp.float32)

    def key_tile(step, accs):
        q_in, g_in = query_grads[step]
        lse_in = later_stats[step][:, :rows]
        delta_in = later_stats[step][:, rows:]
        mask = key_masks[step]
        s = jnp.einsum("hkd,hqd->hkq", key_h, q_in, preferred_element_type=jnp.float32) * scale
        s = jnp.where(mask[None], s, -1e30)
        prob = jnp.where(mask[None], jnp.exp(s - lse_in[:, None, :]), 0.0)
        dprob = jnp.einsum("hkd,hqd->hkq", value_h, g_in, preferred_element_type=jnp.float32)
        dscore = (prob * (dprob - delta_in[:, None, :])).astype(jnp.bfloat16)
        prob_b, dscore = lax.optimization_barrier((prob.astype(jnp.bfloat16), dscore))
        k_part = jnp.einsum("hkq,hqd->hkd", dscore, q_in, preferred_element_type=jnp.float32)
        v_part = jnp.einsum("hkq,hqd->hkd", prob_b, g_in, preferred_element_type=jnp.float32)
        return (accs[0] + k_part, accs[1] + v_part)

    for step in range(1, window):
        query_acc = query_tile(step, query_acc)
        key_acc, value_acc = key_tile(step, (key_acc, value_acc))
    query_grad = from_heads(query_acc * scale).astype(jnp.bfloat16)
    key_grad = from_heads(key_acc * scale).astype(jnp.bfloat16)
    value_grad = from_heads(value_acc).astype(jnp.bfloat16)
    return (query_grad, key_grad, value_grad)


def solution(mesh):
    in_specs = (
        P(("cx", "cy"), None),
        P(("cx", "cy"), None),
        P(("cx", "cy"), None),
        P(("cx", "cy"), None),
        P(("cx", "cy"), None),
        P(),
    )
    out_specs = (P(("cx", "cy"), None), P(("cx", "cy"), None), P(("cx", "cy"), None))
    return jax.shard_map(
        per_device, mesh=mesh, in_specs=in_specs, out_specs=out_specs, check_vma=False
    )
```

```python
import math

import jax
import jax.numpy as jnp
from jax import lax
from jax.sharding import PartitionSpec as P

HEADS = 8
DH = 128
BLOCK = 128
REACH = 7


def from_behind(value, axis, steps):
    count = lax.axis_size(axis)
    first, last = (max(0, -steps), min(count, count - steps))
    return lax.ppermute(value, axis, [(source, source + steps) for source in range(first, last)])


def doc_window(doc_blocks, first_block, count):
    ends = jnp.cumsum(doc_blocks)
    starts = ends - doc_blocks
    block_ids = first_block + jnp.arange(count, dtype=jnp.int32)
    found = jnp.sum((starts[None, :] <= block_ids[:, None]).astype(jnp.int32), axis=1) - 1
    return jnp.where(block_ids >= ends[-1], -2, found)


def per_device(query_rows, key_rows, value_rows, forward_out, out_grad, doc_blocks):
    rows, features = query_rows.shape
    scale = 1.0 / math.sqrt(DH)
    axes = ("cx", "cy")
    shard = lax.axis_index(axes)
    per_shard = rows // BLOCK
    window = REACH + 1
    block_docs = doc_window(doc_blocks, (shard - REACH) * per_shard, (2 * REACH + 1) * per_shard)
    token_docs = jnp.repeat(block_docs, BLOCK)

    def docs_at(step):
        return token_docs[(REACH + step) * rows : (REACH + step + 1) * rows]

    local_docs = docs_at(0)
    offsets = jnp.arange(rows, dtype=jnp.int32)
    causal = offsets[None, :] <= offsets[:, None]
    query_masks = [local_docs[:, None] == docs_at(-step)[None, :] for step in range(window)]
    query_masks[0] = query_masks[0] & causal
    key_masks = [local_docs[:, None] == docs_at(step)[None, :] for step in range(window)]

    def to_heads(x):
        return x.reshape(rows, HEADS, DH).transpose(1, 0, 2)

    def from_heads(x):
        return x.transpose(1, 0, 2).reshape(rows, features)

    query_h = to_heads(query_rows)
    grad_h = to_heads(out_grad)
    key_h = to_heads(key_rows)
    value_h = to_heads(value_rows)
    delta = jnp.einsum(
        "hqd,hqd->hq", grad_h, to_heads(forward_out), preferred_element_type=jnp.float32
    )

    keys_in = [key_h]
    query_grads = [(query_h, grad_h)]
    moving_k = key_h
    moving_qg = (query_h, grad_h)
    for step in range(1, window):
        moving_k = from_behind(moving_k, axes, 1)
        moving_qg = from_behind(moving_qg, axes, -1)
        keys_in.append(moving_k)
        query_grads.append(moving_qg)
    values_in = [value_h]
    moving_v, _ = lax.optimization_barrier((value_h, moving_k))
    for step in range(1, window):
        moving_v = from_behind(moving_v, axes, 1)
        values_in.append(moving_v)
    key_values = list(zip(keys_in, values_in))

    def scores_of(q, k, mask):
        s = jnp.einsum("hqd,hkd->hqk", q, k, preferred_element_type=jnp.float32) * scale
        return jnp.where(mask[None], s, -1e30)

    def tile_stats(q, k, mask):
        s = scores_of(q, k, mask)
        top = jnp.max(s, axis=2)
        return (top, jnp.sum(jnp.exp(s - top[..., None]), axis=2))

    def merged(step, stats):
        part = tile_stats(query_h, keys_in[step], query_masks[step])
        top = jnp.maximum(stats[0], part[0])
        total = stats[1] * jnp.exp(stats[0] - top) + part[1] * jnp.exp(part[0] - top)
        return (top, total)

    stats = tile_stats(query_h, key_h, query_masks[0])
    for step in range(1, window):
        stats = merged(step, stats)
    logsum = stats[0] + jnp.log(stats[1])

    row_stats = jnp.concatenate([logsum, delta], axis=1)
    later_stats = [row_stats] + [from_behind(row_stats, axes, -step) for step in range(1, window)]

    def tile_grads(q, g, k, v, lse, dlt, mask):
        s = scores_of(q, k, mask)
        prob = jnp.where(mask[None], jnp.exp(s - lse[..., None]), 0.0)
        dprob = jnp.einsum("hqd,hkd->hqk", g, v, preferred_element_type=jnp.float32)
        dscore = (prob * (dprob - dlt[..., None])).astype(jnp.bfloat16)
        return prob.astype(jnp.bfloat16), dscore

    prob_b, dscore = lax.optimization_barrier(
        tile_grads(query_h, grad_h, key_h, value_h, logsum, delta, query_masks[0])
    )
    query_acc = jnp.einsum("hqk,hkd->hqd", dscore, key_h, preferred_element_type=jnp.float32)
    key_acc = jnp.einsum("hqk,hqd->hkd", dscore, query_h, preferred_element_type=jnp.float32)
    value_acc = jnp.einsum("hqk,hqd->hkd", prob_b, grad_h, preferred_element_type=jnp.float32)

    def query_tile(step, acc):
        k_in, v_in = key_values[step]
        dscore = lax.optimization_barrier(
            tile_grads(query_h, grad_h, k_in, v_in, logsum, delta, query_masks[step])[1]
        )
        return acc + jnp.einsum("hqk,hkd->hqd", dscore, k_in, preferred_element_type=jnp.float32)

    def key_tile(step, accs):
        q_in, g_in = query_grads[step]
        lse_in = later_stats[step][:, :rows]
        delta_in = later_stats[step][:, rows:]
        mask = key_masks[step]
        s = jnp.einsum("hkd,hqd->hkq", key_h, q_in, preferred_element_type=jnp.float32) * scale
        s = jnp.where(mask[None], s, -1e30)
        prob = jnp.where(mask[None], jnp.exp(s - lse_in[:, None, :]), 0.0)
        dprob = jnp.einsum("hkd,hqd->hkq", value_h, g_in, preferred_element_type=jnp.float32)
        dscore = (prob * (dprob - delta_in[:, None, :])).astype(jnp.bfloat16)
        prob_b, dscore = lax.optimization_barrier((prob.astype(jnp.bfloat16), dscore))
        k_part = jnp.einsum("hkq,hqd->hkd", dscore, q_in, preferred_element_type=jnp.float32)
        v_part = jnp.einsum("hkq,hqd->hkd", prob_b, g_in, preferred_element_type=jnp.float32)
        return (accs[0] + k_part, accs[1] + v_part)

    for step in range(1, window):
        query_acc = query_tile(step, query_acc)
        key_acc, value_acc = key_tile(step, (key_acc, value_acc))
    query_grad = from_heads(query_acc * scale).astype(jnp.bfloat16)
    key_grad = from_heads(key_acc * scale).astype(jnp.bfloat16)
    value_grad = from_heads(value_acc).astype(jnp.bfloat16)
    return (query_grad, key_grad, value_grad)


def solution(mesh):
    in_specs = (
        P(("cx", "cy"), None),
        P(("cx", "cy"), None),
        P(("cx", "cy"), None),
        P(("cx", "cy"), None),
        P(("cx", "cy"), None),
        P(),
    )
    out_specs = (P(("cx", "cy"), None), P(("cx", "cy"), None), P(("cx", "cy"), None))
    return jax.shard_map(
        per_device, mesh=mesh, in_specs=in_specs, out_specs=out_specs, check_vma=False
    )
```

```python
import math

import jax
import jax.numpy as jnp
from jax import lax
from jax.sharding import PartitionSpec as P

HEADS = 8
DH = 128
BLOCK = 128
REACH = 7


def from_behind(value, axis, steps):
    count = lax.axis_size(axis)
    first, last = (max(0, -steps), min(count, count - steps))
    return lax.ppermute(value, axis, [(source, source + steps) for source in range(first, last)])


def doc_window(doc_blocks, first_block, count):
    ends = jnp.cumsum(doc_blocks)
    starts = ends - doc_blocks
    block_ids = first_block + jnp.arange(count, dtype=jnp.int32)
    found = jnp.sum((starts[None, :] <= block_ids[:, None]).astype(jnp.int32), axis=1) - 1
    return jnp.where(block_ids >= ends[-1], -2, found)


def per_device(query_rows, key_rows, value_rows, forward_out, out_grad, doc_blocks):
    rows, features = query_rows.shape
    scale = 1.0 / math.sqrt(DH)
    axes = ("cx", "cy")
    shard = lax.axis_index(axes)
    per_shard = rows // BLOCK
    window = REACH + 1
    block_docs = doc_window(doc_blocks, (shard - REACH) * per_shard, (2 * REACH + 1) * per_shard)
    token_docs = jnp.repeat(block_docs, BLOCK)

    def docs_at(step):
        return token_docs[(REACH + step) * rows : (REACH + step + 1) * rows]

    local_docs = docs_at(0)
    offsets = jnp.arange(rows, dtype=jnp.int32)
    causal = offsets[None, :] <= offsets[:, None]
    query_masks = [local_docs[:, None] == docs_at(-step)[None, :] for step in range(window)]
    query_masks[0] = query_masks[0] & causal
    key_masks = [local_docs[:, None] == docs_at(step)[None, :] for step in range(window)]

    def to_heads(x):
        return x.reshape(rows, HEADS, DH).transpose(1, 0, 2)

    def from_heads(x):
        return x.transpose(1, 0, 2).reshape(rows, features)

    query_h = to_heads(query_rows)
    grad_h = to_heads(out_grad)
    key_h = to_heads(key_rows)
    value_h = to_heads(value_rows)
    delta = jnp.einsum(
        "hqd,hqd->hq", grad_h, to_heads(forward_out), preferred_element_type=jnp.float32
    )

    key_values = [(key_h, value_h)]
    query_grads = [(query_h, grad_h)]
    moving_kv = jnp.stack([key_h, value_h])
    moving_qg = jnp.stack([query_h, grad_h])
    for step in range(1, window):
        moving_kv = from_behind(moving_kv, axes, 1)
        moving_qg = from_behind(moving_qg, axes, -1)
        key_values.append((moving_kv[0], moving_kv[1]))
        query_grads.append((moving_qg[0], moving_qg[1]))

    def scores_of(q, k, mask):
        s = jnp.einsum("hqd,hkd->hqk", q, k, preferred_element_type=jnp.float32) * scale
        return jnp.where(mask[None], s, -1e30)

    def tile_stats(q, k, mask):
        s = scores_of(q, k, mask)
        top = jnp.max(s, axis=2)
        return (top, jnp.sum(jnp.exp(s - top[..., None]), axis=2))

    def merged(step, stats):
        part = tile_stats(query_h, key_values[step][0], query_masks[step])
        top = jnp.maximum(stats[0], part[0])
        total = stats[1] * jnp.exp(stats[0] - top) + part[1] * jnp.exp(part[0] - top)
        return (top, total)

    stats = tile_stats(query_h, key_h, query_masks[0])
    for step in range(1, window):
        stats = merged(step, stats)
    logsum = stats[0] + jnp.log(stats[1])

    row_stats = jnp.concatenate([logsum, delta], axis=1)
    later_stats = [row_stats] + [from_behind(row_stats, axes, -step) for step in range(1, window)]

    def tile_grads(q, g, k, v, lse, dlt, mask):
        s = scores_of(q, k, mask)
        prob = jnp.where(mask[None], jnp.exp(s - lse[..., None]), 0.0)
        dprob = jnp.einsum("hqd,hkd->hqk", g, v, preferred_element_type=jnp.float32)
        dscore = (prob * (dprob - dlt[..., None])).astype(jnp.bfloat16)
        return prob.astype(jnp.bfloat16), dscore

    prob_b, dscore = lax.optimization_barrier(
        tile_grads(query_h, grad_h, key_h, value_h, logsum, delta, query_masks[0])
    )
    query_acc = jnp.einsum("hqk,hkd->hqd", dscore, key_h, preferred_element_type=jnp.float32)
    key_acc = jnp.einsum("hqk,hqd->hkd", dscore, query_h, preferred_element_type=jnp.float32)
    value_acc = jnp.einsum("hqk,hqd->hkd", prob_b, grad_h, preferred_element_type=jnp.float32)

    def query_tile(step, acc):
        k_in, v_in = key_values[step]
        dscore = lax.optimization_barrier(
            tile_grads(query_h, grad_h, k_in, v_in, logsum, delta, query_masks[step])[1]
        )
        return acc + jnp.einsum("hqk,hkd->hqd", dscore, k_in, preferred_element_type=jnp.float32)

    def key_tile(step, accs):
        q_in, g_in = query_grads[step]
        lse_in = later_stats[step][:, :rows]
        delta_in = later_stats[step][:, rows:]
        mask = key_masks[step]
        s = jnp.einsum("hkd,hqd->hkq", key_h, q_in, preferred_element_type=jnp.float32) * scale
        s = jnp.where(mask[None], s, -1e30)
        prob = jnp.where(mask[None], jnp.exp(s - lse_in[:, None, :]), 0.0)
        dprob = jnp.einsum("hkd,hqd->hkq", value_h, g_in, preferred_element_type=jnp.float32)
        dscore = (prob * (dprob - delta_in[:, None, :])).astype(jnp.bfloat16)
        prob_b, dscore = lax.optimization_barrier((prob.astype(jnp.bfloat16), dscore))
        k_part = jnp.einsum("hkq,hqd->hkd", dscore, q_in, preferred_element_type=jnp.float32)
        v_part = jnp.einsum("hkq,hqd->hkd", prob_b, g_in, preferred_element_type=jnp.float32)
        return (accs[0] + k_part, accs[1] + v_part)

    for step in range(1, window):
        query_acc = query_tile(step, query_acc)
        key_acc, value_acc = key_tile(step, (key_acc, value_acc))
    query_grad = from_heads(query_acc * scale).astype(jnp.bfloat16)
    key_grad = from_heads(key_acc * scale).astype(jnp.bfloat16)
    value_grad = from_heads(value_acc).astype(jnp.bfloat16)
    return (query_grad, key_grad, value_grad)


def solution(mesh):
    in_specs = (
        P(("cx", "cy"), None),
        P(("cx", "cy"), None),
        P(("cx", "cy"), None),
        P(("cx", "cy"), None),
        P(("cx", "cy"), None),
        P(),
    )
    out_specs = (P(("cx", "cy"), None), P(("cx", "cy"), None), P(("cx", "cy"), None))
    return jax.shard_map(
        per_device, mesh=mesh, in_specs=in_specs, out_specs=out_specs, check_vma=False
    )
```

```python
import math

import jax
import jax.numpy as jnp
from jax import lax
from jax.sharding import PartitionSpec as P

HEADS = 8
DH = 128
BLOCK = 128
REACH = 7


def from_behind(value, axis, steps):
    count = lax.axis_size(axis)
    first, last = (max(0, -steps), min(count, count - steps))
    return lax.ppermute(value, axis, [(source, source + steps) for source in range(first, last)])


def doc_window(doc_blocks, first_block, count):
    ends = jnp.cumsum(doc_blocks)
    starts = ends - doc_blocks
    block_ids = first_block + jnp.arange(count, dtype=jnp.int32)
    found = jnp.sum((starts[None, :] <= block_ids[:, None]).astype(jnp.int32), axis=1) - 1
    return jnp.where(block_ids >= ends[-1], -2, found)


def per_device(query_rows, key_rows, value_rows, forward_out, out_grad, doc_blocks):
    rows, features = query_rows.shape
    scale = 1.0 / math.sqrt(DH)
    axes = ("cx", "cy")
    shard = lax.axis_index(axes)
    per_shard = rows // BLOCK
    window = REACH + 1
    block_docs = doc_window(doc_blocks, (shard - REACH) * per_shard, (2 * REACH + 1) * per_shard)
    token_docs = jnp.repeat(block_docs, BLOCK)

    def docs_at(step):
        return token_docs[(REACH + step) * rows : (REACH + step + 1) * rows]

    local_docs = docs_at(0)
    offsets = jnp.arange(rows, dtype=jnp.int32)
    causal = offsets[None, :] <= offsets[:, None]
    query_masks = [local_docs[:, None] == docs_at(-step)[None, :] for step in range(window)]
    query_masks[0] = query_masks[0] & causal
    key_masks = [local_docs[:, None] == docs_at(step)[None, :] for step in range(window)]

    def to_heads(x):
        return x.reshape(rows, HEADS, DH).transpose(1, 0, 2)

    def from_heads(x):
        return x.transpose(1, 0, 2).reshape(rows, features)

    query_h = to_heads(query_rows)
    grad_h = to_heads(out_grad)
    key_h = to_heads(key_rows)
    value_h = to_heads(value_rows)
    delta = jnp.einsum(
        "qhd,qhd->hq",
        out_grad.reshape(rows, HEADS, DH),
        forward_out.reshape(rows, HEADS, DH),
        preferred_element_type=jnp.float32,
    )

    key_values = [(key_h, value_h)]
    query_grads = [(query_h, grad_h)]
    moving_kv = (key_h, value_h)
    moving_qg = (query_h, grad_h)
    for step in range(1, window):
        moving_kv = from_behind(moving_kv, axes, 1)
        moving_qg = from_behind(moving_qg, axes, -1)
        key_values.append(moving_kv)
        query_grads.append(moving_qg)

    def scores_of(q, k, mask):
        s = jnp.einsum("hqd,hkd->hqk", q, k, preferred_element_type=jnp.float32) * scale
        return jnp.where(mask[None], s, -1e30)

    def tile_stats(q, k, mask):
        s = scores_of(q, k, mask)
        top = jnp.max(s, axis=2)
        return (top, jnp.sum(jnp.exp(s - top[..., None]), axis=2))

    def merged(step, stats):
        part = tile_stats(query_h, key_values[step][0], query_masks[step])
        top = jnp.maximum(stats[0], part[0])
        total = stats[1] * jnp.exp(stats[0] - top) + part[1] * jnp.exp(part[0] - top)
        return (top, total)

    stats = tile_stats(query_h, key_h, query_masks[0])
    for step in range(1, window):
        stats = merged(step, stats)
    logsum = stats[0] + jnp.log(stats[1])

    row_stats = jnp.concatenate([logsum, delta], axis=1)
    later_stats = [row_stats] + [from_behind(row_stats, axes, -step) for step in range(1, window)]

    def tile_grads(q, g, k, v, lse, dlt, mask):
        s = scores_of(q, k, mask)
        prob = jnp.where(mask[None], jnp.exp(s - lse[..., None]), 0.0)
        dprob = jnp.einsum("hqd,hkd->hqk", g, v, preferred_element_type=jnp.float32)
        dscore = (prob * (dprob - dlt[..., None])).astype(jnp.bfloat16)
        return prob.astype(jnp.bfloat16), dscore

    prob_b, dscore = lax.optimization_barrier(
        tile_grads(query_h, grad_h, key_h, value_h, logsum, delta, query_masks[0])
    )
    query_acc = jnp.einsum("hqk,hkd->hqd", dscore, key_h, preferred_element_type=jnp.float32)
    key_acc = jnp.einsum("hqk,hqd->hkd", dscore, query_h, preferred_element_type=jnp.float32)
    value_acc = jnp.einsum("hqk,hqd->hkd", prob_b, grad_h, preferred_element_type=jnp.float32)

    def query_tile(step, acc):
        k_in, v_in = key_values[step]
        dscore = lax.optimization_barrier(
            tile_grads(query_h, grad_h, k_in, v_in, logsum, delta, query_masks[step])[1]
        )
        return acc + jnp.einsum("hqk,hkd->hqd", dscore, k_in, preferred_element_type=jnp.float32)

    def key_tile(step, accs):
        q_in, g_in = query_grads[step]
        lse_in = later_stats[step][:, :rows]
        delta_in = later_stats[step][:, rows:]
        mask = key_masks[step]
        s = jnp.einsum("hkd,hqd->hkq", key_h, q_in, preferred_element_type=jnp.float32) * scale
        s = jnp.where(mask[None], s, -1e30)
        prob = jnp.where(mask[None], jnp.exp(s - lse_in[:, None, :]), 0.0)
        dprob = jnp.einsum("hkd,hqd->hkq", value_h, g_in, preferred_element_type=jnp.float32)
        dscore = (prob * (dprob - delta_in[:, None, :])).astype(jnp.bfloat16)
        prob_b, dscore = lax.optimization_barrier((prob.astype(jnp.bfloat16), dscore))
        k_part = jnp.einsum("hkq,hqd->hkd", dscore, q_in, preferred_element_type=jnp.float32)
        v_part = jnp.einsum("hkq,hqd->hkd", prob_b, g_in, preferred_element_type=jnp.float32)
        return (accs[0] + k_part, accs[1] + v_part)

    for step in range(1, window):
        query_acc = query_tile(step, query_acc)
        key_acc, value_acc = key_tile(step, (key_acc, value_acc))
    query_grad = from_heads(query_acc * scale).astype(jnp.bfloat16)
    key_grad = from_heads(key_acc * scale).astype(jnp.bfloat16)
    value_grad = from_heads(value_acc).astype(jnp.bfloat16)
    return (query_grad, key_grad, value_grad)


def solution(mesh):
    in_specs = (
        P(("cx", "cy"), None),
        P(("cx", "cy"), None),
        P(("cx", "cy"), None),
        P(("cx", "cy"), None),
        P(("cx", "cy"), None),
        P(),
    )
    out_specs = (P(("cx", "cy"), None), P(("cx", "cy"), None), P(("cx", "cy"), None))
    return jax.shard_map(
        per_device, mesh=mesh, in_specs=in_specs, out_specs=out_specs, check_vma=False
    )
```

```python
import math

import jax
import jax.numpy as jnp
from jax import lax
from jax.sharding import PartitionSpec as P

HEADS = 8
DH = 128
BLOCK = 128
REACH = 7


def from_behind(value, axis, steps):
    count = lax.axis_size(axis)
    first, last = (max(0, -steps), min(count, count - steps))
    return lax.ppermute(value, axis, [(source, source + steps) for source in range(first, last)])


def doc_window(doc_blocks, first_block, count):
    ends = jnp.cumsum(doc_blocks)
    starts = ends - doc_blocks
    block_ids = first_block + jnp.arange(count, dtype=jnp.int32)
    found = jnp.sum((starts[None, :] <= block_ids[:, None]).astype(jnp.int32), axis=1) - 1
    return jnp.where(block_ids >= ends[-1], -2, found)


def per_device(query_rows, key_rows, value_rows, forward_out, out_grad, doc_blocks):
    rows, features = query_rows.shape
    scale = 1.0 / math.sqrt(DH)
    axes = ("cx", "cy")
    shard = lax.axis_index(axes)
    per_shard = rows // BLOCK
    window = REACH + 1
    block_docs = doc_window(doc_blocks, (shard - REACH) * per_shard, (2 * REACH + 1) * per_shard)
    token_docs = jnp.repeat(block_docs, BLOCK)

    def docs_at(step):
        return token_docs[(REACH + step) * rows : (REACH + step + 1) * rows]

    local_docs = docs_at(0)
    offsets = jnp.arange(rows, dtype=jnp.int32)
    causal = offsets[None, :] <= offsets[:, None]
    query_masks = [local_docs[:, None] == docs_at(-step)[None, :] for step in range(window)]
    query_masks[0] = query_masks[0] & causal
    key_masks = [local_docs[:, None] == docs_at(step)[None, :] for step in range(window)]

    def to_heads(x):
        return x.reshape(rows, HEADS, DH).transpose(1, 0, 2)

    def from_heads(x):
        return x.transpose(1, 0, 2).reshape(rows, features)

    query_h = to_heads(query_rows)
    grad_h = to_heads(out_grad)
    key_h = to_heads(key_rows)
    value_h = to_heads(value_rows)
    delta = jnp.einsum(
        "hqd,hqd->hq", grad_h, to_heads(forward_out), preferred_element_type=jnp.float32
    )

    key_values = [(key_h, value_h)]
    query_grads = [(query_h, grad_h)]
    moving_kv = (key_h, value_h)
    moving_qg = (query_h, grad_h)
    for step in range(1, window):
        moving_kv = from_behind(moving_kv, axes, 1)
        moving_qg = from_behind(moving_qg, axes, -1)
        key_values.append(moving_kv)
        query_grads.append(moving_qg)

    def scores_of(q, k, mask):
        s = jnp.einsum("hqd,hkd->hqk", q, k, preferred_element_type=jnp.float32) * scale
        return jnp.where(mask[None], s, -1e30)

    def tile_stats(q, k, mask):
        s = scores_of(q, k, mask)
        top = jnp.max(s, axis=2)
        return (top, jnp.sum(jnp.exp(s - top[..., None]), axis=2))

    def merged(step, stats):
        part = tile_stats(query_h, key_values[step][0], query_masks[step])
        top = jnp.maximum(stats[0], part[0])
        total = stats[1] * jnp.exp(stats[0] - top) + part[1] * jnp.exp(part[0] - top)
        return (top, total)

    stats = tile_stats(query_h, key_h, query_masks[0])
    for step in range(1, window):
        stats = merged(step, stats)
    logsum = stats[0] + jnp.log(stats[1])

    row_stats = jnp.concatenate([logsum, delta], axis=1)
    later_stats = [row_stats] + [from_behind(row_stats, axes, -step) for step in range(1, window)]

    def tile_grads(q, g, k, v, lse, dlt, mask):
        s = scores_of(q, k, mask)
        prob = jnp.where(mask[None], jnp.exp(s - lse[..., None]), 0.0)
        dprob = jnp.einsum("hqd,hkd->hqk", g, v, preferred_element_type=jnp.float32)
        dscore = (prob * (dprob - dlt[..., None])).astype(jnp.bfloat16)
        return prob.astype(jnp.bfloat16), dscore

    prob_b, dscore = lax.optimization_barrier(
        tile_grads(query_h, grad_h, key_h, value_h, logsum, delta, query_masks[0])
    )
    query_acc = jnp.einsum("hqk,hkd->hqd", dscore, key_h, preferred_element_type=jnp.float32)
    key_acc = jnp.einsum("hqk,hqd->hkd", dscore, query_h, preferred_element_type=jnp.float32)
    value_acc = jnp.einsum("hqk,hqd->hkd", prob_b, grad_h, preferred_element_type=jnp.float32)

    def query_tile(step, acc):
        k_in, v_in = key_values[step]
        dscore = tile_grads(query_h, grad_h, k_in, v_in, logsum, delta, query_masks[step])[1]
        return acc + jnp.einsum("hqk,hkd->hqd", dscore, k_in, preferred_element_type=jnp.float32)

    def key_tile(step, accs):
        q_in, g_in = query_grads[step]
        lse_in = later_stats[step][:, :rows]
        delta_in = later_stats[step][:, rows:]
        mask = key_masks[step]
        s = jnp.einsum("hkd,hqd->hkq", key_h, q_in, preferred_element_type=jnp.float32) * scale
        s = jnp.where(mask[None], s, -1e30)
        prob = jnp.where(mask[None], jnp.exp(s - lse_in[:, None, :]), 0.0)
        dprob = jnp.einsum("hkd,hqd->hkq", value_h, g_in, preferred_element_type=jnp.float32)
        dscore = (prob * (dprob - delta_in[:, None, :])).astype(jnp.bfloat16)
        prob_b, dscore = lax.optimization_barrier((prob.astype(jnp.bfloat16), dscore))
        k_part = jnp.einsum("hkq,hqd->hkd", dscore, q_in, preferred_element_type=jnp.float32)
        v_part = jnp.einsum("hkq,hqd->hkd", prob_b, g_in, preferred_element_type=jnp.float32)
        return (accs[0] + k_part, accs[1] + v_part)

    for step in range(1, window):
        query_acc = query_tile(step, query_acc)
        key_acc, value_acc = key_tile(step, (key_acc, value_acc))
    query_grad = from_heads(query_acc * scale).astype(jnp.bfloat16)
    key_grad = from_heads(key_acc * scale).astype(jnp.bfloat16)
    value_grad = from_heads(value_acc).astype(jnp.bfloat16)
    return (query_grad, key_grad, value_grad)


def solution(mesh):
    in_specs = (
        P(("cx", "cy"), None),
        P(("cx", "cy"), None),
        P(("cx", "cy"), None),
        P(("cx", "cy"), None),
        P(("cx", "cy"), None),
        P(),
    )
    out_specs = (P(("cx", "cy"), None), P(("cx", "cy"), None), P(("cx", "cy"), None))
    return jax.shard_map(
        per_device, mesh=mesh, in_specs=in_specs, out_specs=out_specs, check_vma=False
    )
```
